512 devices in a mesh: rep: 8 (over y_hi, core), tp: 64 (over x, z, y_lo).
Axes of the slice: x: 4, y: 8 (y_hi: 4, y_lo: 2; y = y_hi * 2 + y_lo), z: 8, core: 2. Of those that a mesh axis runs over, the one named last changes fastest.
Arguments:
- tokens: bfloat16 [4096, 6144], P(('rep', 'tp')), parts along dimension 0, may hold values from -6 to 6
- ln_gain: bfloat16 [6144], replicated, may hold values from 0.5 to 1.5
- ln_bias: bfloat16 [6144], replicated, may hold values from -4 to 4
- w_qkv: bfloat16 [6144, 18432], P(None, 'tp'), may hold values from -0.078125 to 0.078125
- b_qkv: bfloat16 [18432], P('tp'), may hold values from -6 to 6
- w_dense: bfloat16 [6144, 6144], P(None, 'tp'), may hold values from -0.625 to 0.625
- b_dense: bfloat16 [6144], replicated, may hold values from -6 to 6
- prefix_kv: bfloat16 [2, 32, 128, 6144], P(None, 'rep', None, 'tp'), parts along dimension 1, may hold values from -110 to 110
- decode_kv: bfloat16 [2, 256, 16, 6144], P(None, 'rep', None, 'tp'), parts along dimension 1, may hold values from -110 to 110
- prefix_lens: int32 [32], P('rep'), parts along dimension 0, may hold values from 0 to 128, as said below
- span_request: int32 [32], P('rep'), parts along dimension 0, may hold values from 0 to 3, each once
- decode_lens: int32 [256], P('rep'), parts along dimension 0, may hold values from 1 to 16, 256 in all
- slot_valid: int32 [256, 16], P('rep'), parts along dimension 0, may hold values 0 or 1
Outputs:
- layer_out: bfloat16 [4096, 6144], P(('rep', 'tp')), parts along dimension 0
The draws below stay inside these ranges and needn't reach their ends.
There are 8 independent parts, one for each index of `rep`. The reference program is written for one: setup_inputs(seed, part) draws one part's arguments, and reference() takes and returns one part's arrays. A program takes and returns all parts, laid end to end along the dimension named above; an argument that names none is the same for every part. Nothing has to cross between parts.
Inputs may be any that keep to these rules, and one draw needn't show every extreme that they name: `prefix_lens`: some request slot has exactly 128 cached tokens. `span_request`: each request slot is continued by exactly one span. `decode_lens`: the lengths sum to 256 and one equals 16.
All inputs are finite; a program needn't handle non-finite values.
Results may differ from the reference program's by a relative error of at most 0.012.
The reference program's roundings to bfloat16 on the way count: a program that leaves them out, or rounds other values in their place, can miss the bound.
Values may be sent and summed in bfloat16 or wider, within the bound.
No kernel may reach another device: no remote copies, remote signals or barrier semaphores. Data moves between devices by JAX's collectives and lax.ppermute only.
A program may use at most 64 MiB of HBM per device.

```python
import math
import jax
import jax.numpy as jnp
import numpy as np
from jax import lax

D = 6144
HS = 96
ROT = 24
HEADS = 64
HD = 6144
TOKENS = 512
NCH = 4
NDEC = 32
CLEN = 120
PMAX = 128
DMAX = 16


def cache_field(key, shape):
    base_key = jax.random.fold_in(key, 0)
    field = jnp.clip(jax.random.normal(base_key, shape, jnp.float32), -4.0, 4.0)
    return field.astype(jnp.bfloat16)


def draw_prefix_kv(key, part):
    return cache_field(jax.random.fold_in(key, 11), (2, NCH, PMAX, HD))


def draw_decode_kv(key, part):
    return cache_field(jax.random.fold_in(key, 13), (2, NDEC, DMAX, HD))


def draw_prefix_lens(key, part):
    lens_key, pick_key = jax.random.split(jax.random.fold_in(key, 5))
    drawn = jax.random.randint(lens_key, (NCH,), 0, PMAX + 1, jnp.int32)
    chosen = jax.random.randint(pick_key, (), 0, NCH, jnp.int32)
    return jnp.where(jnp.arange(NCH, dtype=jnp.int32) == chosen, PMAX, drawn).astype(jnp.int32)


def set_ends(values, stream_key, least, largest):
    spot = [jax.random.randint(jax.random.fold_in(stream_key, axis), (), 0, length) for axis, length in enumerate(values.shape)]
    main_axis = values.shape.index(max(values.shape))
    neighbour = spot[:main_axis] + [(spot[main_axis] + 1) % values.shape[main_axis]] + spot[main_axis + 1:]
    return values.at[tuple(spot)].set(least).at[tuple(neighbour)].set(largest)


def level_of(stream_key, shape, cuts, smallest, largest):
    level, own = 1.0, jax.random.fold_in(stream_key, 6)
    for dim, parts in cuts:
        heights = jnp.exp(jax.random.uniform(jax.random.fold_in(own, dim), (parts,), jnp.float32, smallest / len(cuts), largest / len(cuts)))
        level = level * jnp.repeat(heights, shape[dim] // parts).reshape([-1 if axis == dim else 1 for axis in range(len(shape))])
    return level


def split_up(number_of, total, bound, slope):
    portions = [(1 << 20) // math.isqrt(standing ** slope) + 1 for standing in range(2, number_of + 1)]
    rest, counts = total - bound - (number_of - 1), [1] * (number_of - 1)
    while rest > 0:
        free = [i for i in range(number_of - 1) if counts[i] < bound]
        mass, budget = sum([portions[i] for i in free]), rest
        for i in free:
            extra = min(bound - counts[i], max(1, budget * portions[i] // mass), rest)
            counts[i] = counts[i] + extra
            rest = rest - extra
    return np.array([bound] + counts)


def uneven(key, count, total, reach, lean):
    if count == 2:
        one = jax.random.randint(key, (), max(1, total - reach), min(reach, total - 1) + 1)
        return jnp.stack([one, total - one])
    lengths = jnp.asarray(split_up(count, total, reach, lean), jnp.int32)
    couples = (count - 1) // 2
    giver, sink = lengths[1:1 + 2 * couples:2], lengths[2:2 + 2 * couples:2]
    margin = jnp.minimum(giver - 1, reach - sink)
    passed = jax.random.randint(jax.random.fold_in(key, 1), (couples,), 0, 1 << 20) % (margin + 1)
    lengths = lengths.at[1:1 + 2 * couples:2].set(giver - passed).at[2:2 + 2 * couples:2].set(sink + passed)
    return lengths[jax.random.permutation(jax.random.fold_in(key, 2), count)]


def bell_draw(stream_key, extent, scale, reach, cuts=(), kind=jnp.bfloat16):
    level = level_of(stream_key, extent, cuts, -0.22, 0.18) if cuts else 1.0
    result = jax.random.normal(stream_key, extent, jnp.float32) * scale * level
    return jnp.minimum(jnp.maximum(result, -reach), reach).astype(kind)


def setup_inputs(seed: int = 0, part: int = 0) -> dict:
    key_of = jax.random.split(jax.random.key(seed), 14)
    part_splits = jax.random.split(jax.random.fold_in(key_of[13], part), 14)
    return {
        "tokens": bell_draw(part_splits[0], (TOKENS, D), 1.0, 6.0, ((0, 64),)),
        "ln_gain": jnp.clip(1.0 + 0.1 * jax.random.normal(key_of[1], (D,), jnp.float32), 0.5, 1.5).astype(jnp.bfloat16),
        "ln_bias": bell_draw(key_of[2], (D,), 0.3, 4.0),
        "w_qkv": bell_draw(key_of[3], (D, 3 * HD), D ** -0.5, 0.078125, ((1, 64),)),
        "b_qkv": bell_draw(key_of[4], (3 * HD,), 0.5, 6.0, ((0, 64),)),
        "w_dense": bell_draw(key_of[5], (HD, D), 0.04, 0.625, ((1, 64),)),
        "b_dense": bell_draw(key_of[6], (D,), 0.5, 6.0),
        "prefix_kv": draw_prefix_kv(jax.random.fold_in(jax.random.fold_in(key_of[13], part), 71), part),
        "decode_kv": draw_decode_kv(jax.random.fold_in(jax.random.fold_in(key_of[13], part), 71), part),
        "prefix_lens": draw_prefix_lens(jax.random.fold_in(jax.random.fold_in(key_of[13], part), 71), part),
        "span_request": jax.random.permutation(part_splits[10], NCH).astype(jnp.int32),
        "decode_lens": uneven(part_splits[11], NDEC, NDEC * DMAX // 2, DMAX, 2).astype(jnp.int32),
        "slot_valid": set_ends((jax.random.randint(part_splits[12], (NDEC, DMAX), 0, 8) < 7).astype(jnp.int32), jax.random.fold_in(part_splits[12], 1), 0, 1),
    }


def layer_norm(rows, gain, shift):
    value_matrix = rows.astype(jnp.float32)
    center = value_matrix - lax.optimization_barrier(jnp.mean(value_matrix, axis=-1, keepdims=True))
    spread = lax.optimization_barrier(jnp.mean(center * center, axis=-1, keepdims=True))
    scaled = center * lax.rsqrt(spread + 1e-05)
    return (scaled * gain.astype(jnp.float32) + shift.astype(jnp.float32)).astype(jnp.bfloat16)

def rotary_tables(places, rot_dims):
    counter = jnp.arange(rot_dims // 2, dtype=jnp.float32)
    inverse = jnp.exp(counter * (-2.0 * math.log(10000.0) / rot_dims))
    angles = places.astype(jnp.float32)[:, None] * inverse[None, :]
    return (jnp.cos(angles), jnp.sin(angles))

def rotate(field, cosine, sine):
    half = cosine.shape[-1]
    first = field[..., :half]
    second = field[..., half:2 * half]
    return jnp.concatenate([first * cosine - second * sine, second * cosine + first * sine, field[..., 2 * half:]], axis=-1)

def token_places(span_lens, cache_lens, span_rows):
    within = jnp.arange(span_rows, dtype=jnp.int32)
    prefill = (span_lens[:, None] + within[None, :]).reshape(-1)
    return jnp.concatenate([prefill, cache_lens]).astype(jnp.int32)

def batch_stacked(form, left, right):
    return jnp.einsum(form, left.astype(jnp.float32), right.astype(jnp.float32))

def attend(logit_scores, live, value_matrix):
    peaks = lax.optimization_barrier(jnp.max(jnp.where(live, logit_scores, -1e+30), axis=-1, keepdims=True))
    raised = jnp.where(live, jnp.exp(logit_scores - peaks), 0.0)
    softmax_weights = (raised / lax.optimization_barrier(jnp.sum(raised, axis=-1, keepdims=True))).astype(jnp.bfloat16)
    return batch_stacked('lsw,lwe->lse', softmax_weights, value_matrix).astype(jnp.bfloat16)

def prefill_attention(query, keys, value_matrix, prefix_keys, prefix_vals, span_lens, decode_rows, score_scale):
    spans = prefix_keys.shape[0]
    slots = prefix_keys.shape[1]
    span_rows = (query.shape[0] - decode_rows) // spans
    prefill_rows = spans * span_rows
    head = query.shape[-1]
    prefill_query_span = query[:prefill_rows].reshape(spans, span_rows, head)
    combined_key_rows = jnp.concatenate([prefix_keys, keys[:prefill_rows].reshape(spans, span_rows, head)], axis=1)
    all_vals = jnp.concatenate([prefix_vals, value_matrix[:prefill_rows].reshape(spans, span_rows, head)], axis=1)
    logit_scores = batch_stacked('jrf,jyf->jry', prefill_query_span, combined_key_rows) * score_scale
    column = jnp.arange(slots + span_rows, dtype=jnp.int32)[None, None, :]
    row_index = jnp.arange(span_rows, dtype=jnp.int32)[None, :, None]
    live = jnp.where(column < slots, column < span_lens[:, None, None], column - slots <= row_index)
    return attend(logit_scores, live, all_vals).reshape(prefill_rows, head)

def decode_attention(query, keys, value_matrix, stored_key_cache, cache_vals, cache_lens, slot_valid, score_scale):
    decode_rows = stored_key_cache.shape[0]
    slots = stored_key_cache.shape[1]
    first_row = query.shape[0] - decode_rows
    decode_query_row = query[first_row:]
    own_keys = keys[first_row:]
    own_vals = value_matrix[first_row:]
    cache_present = batch_stacked('jrf,jyf->jry', decode_query_row[:, None, :], stored_key_cache) * score_scale
    itself = lax.optimization_barrier(jnp.sum(decode_query_row.astype(jnp.float32) * own_keys.astype(jnp.float32), axis=-1))[:, None, None] * score_scale
    logit_scores = jnp.concatenate([cache_present, itself], axis=-1)
    column = jnp.arange(slots, dtype=jnp.int32)[None, :]
    live_cache = (column < cache_lens[:, None]) & (slot_valid == 1)
    live = jnp.concatenate([live_cache, jnp.ones((decode_rows, 1), dtype=bool)], axis=-1)[:, None, :]
    all_vals = jnp.concatenate([cache_vals, own_vals[:, None, :]], axis=1)
    return attend(logit_scores, live, all_vals)[:, 0, :]

def reference(tokens, ln_gain, ln_bias, w_qkv, b_qkv, w_dense, b_dense, prefix_kv, decode_kv, prefix_lens, span_request, decode_lens, slot_valid):
    normed = layer_norm(tokens, ln_gain, ln_bias)
    joined = jnp.dot(normed, w_qkv, preferred_element_type=jnp.float32) + b_qkv.astype(jnp.float32)
    joined = joined.reshape(TOKENS, HEADS, 3, HS)
    span_lens = jnp.take(prefix_lens, span_request, axis=0)
    cosine, sine = rotary_tables(token_places(span_lens, decode_lens, CLEN), ROT)
    query = rotate(joined[:, :, 0, :], cosine[:, None, :], sine[:, None, :]).astype(jnp.bfloat16).reshape(TOKENS, HD)
    keys = rotate(joined[:, :, 1, :], cosine[:, None, :], sine[:, None, :]).astype(jnp.bfloat16).reshape(TOKENS, HD)
    value_matrix = joined[:, :, 2, :].astype(jnp.bfloat16).reshape(TOKENS, HD)
    prefix_keys = jnp.take(prefix_kv[0], span_request, axis=0)
    prefix_vals = jnp.take(prefix_kv[1], span_request, axis=0)
    score_scale = 1.0 / math.sqrt(HS)

    def one_head(head):
        offset = head * HS

        def head_cut(array):
            return lax.dynamic_slice_in_dim(array, offset, HS, array.ndim - 1)
        early = prefill_attention(head_cut(query), head_cut(keys), head_cut(value_matrix), head_cut(prefix_keys), head_cut(prefix_vals), span_lens, NDEC, score_scale)
        late = decode_attention(head_cut(query), head_cut(keys), head_cut(value_matrix), head_cut(decode_kv[0]), head_cut(decode_kv[1]), decode_lens, slot_valid, score_scale)
        return jnp.concatenate([early, late], axis=0)
    stacked = lax.map(one_head, jnp.arange(HEADS, dtype=jnp.int32))
    heads_out = jnp.transpose(stacked, (1, 0, 2)).reshape(TOKENS, HD)
    mixed = jnp.dot(heads_out, w_dense, preferred_element_type=jnp.float32)
    attn = (mixed + b_dense.astype(jnp.float32)).astype(jnp.bfloat16)
    return (attn.astype(jnp.float32) + tokens.astype(jnp.float32)).astype(jnp.bfloat16)
```

```python
import math

import jax
import jax.numpy as jnp
from jax import lax
from jax.sharding import PartitionSpec as P

ROT = 24


def layer_norm(rows, gain, shift):
    value_matrix = rows.astype(jnp.float32)
    center = value_matrix - jnp.mean(value_matrix, axis=-1, keepdims=True)
    spread = jnp.mean(center * center, axis=-1, keepdims=True)
    scaled = center * lax.rsqrt(spread + 1e-05)
    return (scaled * gain.astype(jnp.float32) + shift.astype(jnp.float32)).astype(jnp.bfloat16)


def rotary_tables(places, rot_dims):
    counter = jnp.arange(rot_dims // 2, dtype=jnp.float32)
    inverse = jnp.exp(counter * (-2.0 * math.log(10000.0) / rot_dims))
    angles = places.astype(jnp.float32)[:, None] * inverse[None, :]
    return (jnp.cos(angles), jnp.sin(angles))


def rotate(field, cosine, sine):
    half = cosine.shape[-1]
    first = field[..., :half]
    second = field[..., half : 2 * half]
    return jnp.concatenate(
        [first * cosine - second * sine, second * cosine + first * sine, field[..., 2 * half :]],
        axis=-1,
    )


def token_places(span_lens, cache_lens, span_rows):
    within = jnp.arange(span_rows, dtype=jnp.int32)
    prefill = (span_lens[:, None] + within[None, :]).reshape(-1)
    return jnp.concatenate([prefill, cache_lens])


def batch_stacked(form, left, right):
    return jnp.einsum(form, left, right, preferred_element_type=jnp.float32)


def attend(logit_scores, live, value_matrix):
    peaks = jnp.max(jnp.where(live, logit_scores, -1e30), axis=-1, keepdims=True)
    raised = jnp.where(live, jnp.exp(logit_scores - peaks), 0.0)
    softmax_weights = (raised / jnp.sum(raised, axis=-1, keepdims=True)).astype(jnp.bfloat16)
    return batch_stacked("lsw,lwe->lse", softmax_weights, value_matrix).astype(jnp.bfloat16)


def prefill_attention(
    query, keys, value_matrix, prefix_keys, prefix_vals, span_lens, decode_rows, score_scale
):
    spans = prefix_keys.shape[0]
    slots = prefix_keys.shape[1]
    span_rows = (query.shape[0] - decode_rows) // spans
    prefill_rows = spans * span_rows
    head = query.shape[-1]
    prefill_query_span = query[:prefill_rows].reshape(spans, span_rows, head)
    combined_key_rows = jnp.concatenate(
        [prefix_keys, keys[:prefill_rows].reshape(spans, span_rows, head)], axis=1
    )
    all_vals = jnp.concatenate(
        [prefix_vals, value_matrix[:prefill_rows].reshape(spans, span_rows, head)], axis=1
    )
    logit_scores = (
        batch_stacked("jrf,jyf->jry", prefill_query_span, combined_key_rows) * score_scale
    )
    column = jnp.arange(slots + span_rows, dtype=jnp.int32)[None, None, :]
    row_index = jnp.arange(span_rows, dtype=jnp.int32)[None, :, None]
    live = jnp.where(column < slots, column < span_lens[:, None, None], column - slots <= row_index)
    return attend(logit_scores, live, all_vals).reshape(prefill_rows, head)


def decode_attention(
    query, keys, value_matrix, stored_key_cache, cache_vals, cache_lens, slot_valid, score_scale
):
    decode_rows = stored_key_cache.shape[0]
    slots = stored_key_cache.shape[1]
    first_row = query.shape[0] - decode_rows
    decode_query_row = query[first_row:]
    own_keys = keys[first_row:]
    own_vals = value_matrix[first_row:]
    cache_present = (
        batch_stacked("jrf,jyf->jry", decode_query_row[:, None, :], stored_key_cache) * score_scale
    )
    itself = (
        jnp.sum(decode_query_row.astype(jnp.float32) * own_keys.astype(jnp.float32), axis=-1)[
            :, None, None
        ]
        * score_scale
    )
    logit_scores = jnp.concatenate([cache_present, itself], axis=-1)
    column = jnp.arange(slots, dtype=jnp.int32)[None, :]
    live_cache = (column < cache_lens[:, None]) & (slot_valid == 1)
    live = jnp.concatenate([live_cache, jnp.ones((decode_rows, 1), dtype=bool)], axis=-1)[
        :, None, :
    ]
    all_vals = jnp.concatenate([cache_vals, own_vals[:, None, :]], axis=1)
    return attend(logit_scores, live, all_vals)[:, 0, :]


TP = ("x", "z", "yl")


def gather_rows(block):
    pair = lax.all_gather(block, "yl", axis=0, tiled=True)
    return lax.all_gather(pair, ("x", "z"), axis=0, tiled=True)


def gather_heads(block):
    pair = lax.all_gather(block, "yl", axis=0, tiled=False)
    every = lax.all_gather(pair, ("x", "z"), axis=0, tiled=False)
    return every.reshape((-1,) + block.shape)


def on_device(
    tokens,
    ln_gain,
    ln_bias,
    w_qkv,
    b_qkv,
    w_dense,
    b_dense,
    prefix_kv,
    decode_kv,
    prefix_lens,
    span_request,
    decode_lens,
    slot_valid,
):
    normed = layer_norm(tokens, ln_gain, ln_bias)
    joined = jnp.dot(gather_rows(normed), w_qkv, preferred_element_type=jnp.float32)
    joined = joined + b_qkv.astype(jnp.float32)
    head = joined.shape[1] // 3
    token_count = joined.shape[0]
    spans = prefix_kv.shape[1]
    decode_rows = decode_kv.shape[1]
    span_rows = (token_count - decode_rows) // spans
    span_lens = jnp.take(prefix_lens, span_request, axis=0)
    cosine, sine = rotary_tables(token_places(span_lens, decode_lens, span_rows), ROT)
    query = rotate(joined[:, :head], cosine, sine).astype(jnp.bfloat16)
    keys = rotate(joined[:, head : 2 * head], cosine, sine).astype(jnp.bfloat16)
    value_matrix = joined[:, 2 * head :].astype(jnp.bfloat16)
    prefix_keys = jnp.take(prefix_kv[0], span_request, axis=0)
    prefix_vals = jnp.take(prefix_kv[1], span_request, axis=0)
    score_scale = 1.0 / math.sqrt(head)
    early = prefill_attention(
        query, keys, value_matrix, prefix_keys, prefix_vals, span_lens, decode_rows, score_scale
    )
    late = decode_attention(
        query, keys, value_matrix, decode_kv[0], decode_kv[1], decode_lens, slot_valid, score_scale
    )
    heads_out = jnp.concatenate([early, late], axis=0)
    every_head = gather_heads(heads_out)
    heads = every_head.shape[0]
    mixed = lax.dot_general(
        every_head,
        w_dense.reshape(heads, head, w_dense.shape[1]),
        (((0, 2), (0, 1)), ((), ())),
        preferred_element_type=jnp.float32,
    )
    attn = (mixed + b_dense_own(b_dense, mixed.shape[1])).astype(jnp.bfloat16)
    own_rows = lax.all_to_all(attn, TP, split_axis=0, concat_axis=1, tiled=True)
    return (own_rows.astype(jnp.float32) + tokens.astype(jnp.float32)).astype(jnp.bfloat16)


def b_dense_own(b_dense, width):
    start = lax.axis_index(TP) * width
    return lax.dynamic_slice_in_dim(b_dense, start, width).astype(jnp.float32)


def solution(mesh):
    reps = mesh.shape["rep"]
    coords = [d.coords for d in mesh.devices[0]]
    x_size = len({c[0] for c in coords})
    z_size = len({c[2] for c in coords})
    devices = mesh.devices.reshape(reps, x_size, z_size, -1)
    mesh = jax.sharding.Mesh(devices, ("rep",) + TP)
    placed = (
        P(("rep",) + TP, None),
        P(),
        P(),
        P(None, TP),
        P(TP),
        P(None, TP),
        P(),
        P(None, "rep", None, TP),
        P(None, "rep", None, TP),
        P("rep"),
        P("rep"),
        P("rep"),
        P("rep", None),
    )
    return jax.shard_map(
        on_device, mesh=mesh, in_specs=placed, out_specs=P(("rep",) + TP, None), check_vma=False
    )
```

```python
import math

import jax
import jax.numpy as jnp
from jax import lax
from jax.sharding import PartitionSpec as P

ROT = 24


def layer_norm(rows, gain, shift):
    value_matrix = rows.astype(jnp.float32)
    center = value_matrix - jnp.mean(value_matrix, axis=-1, keepdims=True)
    spread = jnp.mean(center * center, axis=-1, keepdims=True)
    scaled = center * lax.rsqrt(spread + 1e-05)
    return (scaled * gain.astype(jnp.float32) + shift.astype(jnp.float32)).astype(jnp.bfloat16)


def rotary_tables(places, rot_dims):
    counter = jnp.arange(rot_dims // 2, dtype=jnp.float32)
    inverse = jnp.exp(counter * (-2.0 * math.log(10000.0) / rot_dims))
    angles = places.astype(jnp.float32)[:, None] * inverse[None, :]
    return (jnp.cos(angles), jnp.sin(angles))


def rotate(field, cosine, sine):
    half = cosine.shape[-1]
    first = field[..., :half]
    second = field[..., half : 2 * half]
    return jnp.concatenate(
        [first * cosine - second * sine, second * cosine + first * sine, field[..., 2 * half :]],
        axis=-1,
    )


def token_places(span_lens, cache_lens, span_rows):
    within = jnp.arange(span_rows, dtype=jnp.int32)
    prefill = (span_lens[:, None] + within[None, :]).reshape(-1)
    return jnp.concatenate([prefill, cache_lens])


def batch_stacked(form, left, right):
    return jnp.einsum(form, left, right, preferred_element_type=jnp.float32)


def attend(logit_scores, live, value_matrix):
    peaks = jnp.max(jnp.where(live, logit_scores, -1e30), axis=-1, keepdims=True)
    raised = jnp.where(live, jnp.exp(logit_scores - peaks), 0.0)
    softmax_weights = (raised / jnp.sum(raised, axis=-1, keepdims=True)).astype(jnp.bfloat16)
    return batch_stacked("lsw,lwe->lse", softmax_weights, value_matrix).astype(jnp.bfloat16)


def prefill_attention(
    query, keys, value_matrix, prefix_keys, prefix_vals, span_lens, decode_rows, score_scale
):
    spans = prefix_keys.shape[0]
    slots = prefix_keys.shape[1]
    span_rows = (query.shape[0] - decode_rows) // spans
    prefill_rows = spans * span_rows
    head = query.shape[-1]
    prefill_query_span = query[:prefill_rows].reshape(spans, span_rows, head)
    combined_key_rows = jnp.concatenate(
        [prefix_keys, keys[:prefill_rows].reshape(spans, span_rows, head)], axis=1
    )
    all_vals = jnp.concatenate(
        [prefix_vals, value_matrix[:prefill_rows].reshape(spans, span_rows, head)], axis=1
    )
    logit_scores = (
        batch_stacked("jrf,jyf->jry", prefill_query_span, combined_key_rows) * score_scale
    )
    column = jnp.arange(slots + span_rows, dtype=jnp.int32)[None, None, :]
    row_index = jnp.arange(span_rows, dtype=jnp.int32)[None, :, None]
    live = jnp.where(column < slots, column < span_lens[:, None, None], column - slots <= row_index)
    return attend(logit_scores, live, all_vals).reshape(prefill_rows, head)


def decode_attention(
    query, keys, value_matrix, stored_key_cache, cache_vals, cache_lens, slot_valid, score_scale
):
    decode_rows = stored_key_cache.shape[0]
    slots = stored_key_cache.shape[1]
    first_row = query.shape[0] - decode_rows
    decode_query_row = query[first_row:]
    own_keys = keys[first_row:]
    own_vals = value_matrix[first_row:]
    cache_present = (
        batch_stacked("jrf,jyf->jry", decode_query_row[:, None, :], stored_key_cache) * score_scale
    )
    itself = (
        jnp.sum(decode_query_row.astype(jnp.float32) * own_keys.astype(jnp.float32), axis=-1)[
            :, None, None
        ]
        * score_scale
    )
    logit_scores = jnp.concatenate([cache_present, itself], axis=-1)
    column = jnp.arange(slots, dtype=jnp.int32)[None, :]
    live_cache = (column < cache_lens[:, None]) & (slot_valid == 1)
    live = jnp.concatenate([live_cache, jnp.ones((decode_rows, 1), dtype=bool)], axis=-1)[
        :, None, :
    ]
    all_vals = jnp.concatenate([cache_vals, own_vals[:, None, :]], axis=1)
    return attend(logit_scores, live, all_vals)[:, 0, :]


TP = ("x", "z", "yl")


def gather_rows(block):
    pair = lax.all_gather(block, "yl", axis=0, tiled=True)
    return lax.all_gather(pair, ("x", "z"), axis=0, tiled=True)


def gather_heads(block):
    pair = lax.all_gather(block, "yl", axis=0, tiled=False)
    every = lax.all_gather(pair, ("x", "z"), axis=0, tiled=False)
    return every.reshape((-1,) + block.shape)


def on_device(
    tokens,
    ln_gain,
    ln_bias,
    w_qkv,
    b_qkv,
    w_dense,
    b_dense,
    prefix_kv,
    decode_kv,
    prefix_lens,
    span_request,
    decode_lens,
    slot_valid,
):
    normed = layer_norm(tokens, ln_gain, ln_bias)
    joined = jnp.dot(gather_rows(normed), w_qkv, preferred_element_type=jnp.float32)
    joined = joined + b_qkv.astype(jnp.float32)
    head = joined.shape[1] // 3
    token_count = joined.shape[0]
    spans = prefix_kv.shape[1]
    decode_rows = decode_kv.shape[1]
    span_rows = (token_count - decode_rows) // spans
    span_lens = jnp.take(prefix_lens, span_request, axis=0)
    cosine, sine = rotary_tables(token_places(span_lens, decode_lens, span_rows), ROT)
    query = rotate(joined[:, :head], cosine, sine).astype(jnp.bfloat16)
    keys = rotate(joined[:, head : 2 * head], cosine, sine).astype(jnp.bfloat16)
    value_matrix = joined[:, 2 * head :].astype(jnp.bfloat16)
    prefix_keys = jnp.take(prefix_kv[0], span_request, axis=0)
    prefix_vals = jnp.take(prefix_kv[1], span_request, axis=0)
    score_scale = 1.0 / math.sqrt(head)
    early = prefill_attention(
        query, keys, value_matrix, prefix_keys, prefix_vals, span_lens, decode_rows, score_scale
    )
    late = decode_attention(
        query, keys, value_matrix, decode_kv[0], decode_kv[1], decode_lens, slot_valid, score_scale
    )
    heads_out = jnp.concatenate([early, late], axis=0)
    attn = dense_in_pairs(heads_out, w_dense, b_dense)
    return (attn.astype(jnp.float32) + tokens.astype(jnp.float32)).astype(jnp.bfloat16)


def dense_in_pairs(heads_out, w_dense, b_dense):
    partner = [(0, 1), (1, 0)]
    side = lax.axis_index("yl")
    rows, head = heads_out.shape
    width = w_dense.shape[1]
    groups = lax.axis_index(("x", "z"))
    per_device = rows // (2 * lax.axis_size(("x", "z")))
    other_w = lax.ppermute(w_dense, "yl", partner)
    by_owner = heads_out.reshape(-1, 2, per_device, head)
    mine = lax.dynamic_index_in_dim(by_owner, side, axis=1, keepdims=False)
    theirs = lax.dynamic_index_in_dim(by_owner, 1 - side, axis=1, keepdims=False)
    got = lax.ppermute(theirs, "yl", partner)
    pair_heads = jnp.stack([mine, got], axis=1)
    pair_heads = jnp.where(side == 0, pair_heads, pair_heads[:, ::-1])
    every = lax.all_gather(pair_heads, ("x", "z"), axis=0, tiled=False)
    pairs = every.shape[0]
    w_pair = jnp.stack([w_dense, other_w]).reshape(2, pairs, 2, head, width)
    mixed = lax.dot_general(
        every,
        w_pair,
        (((0, 2, 4), (1, 2, 3)), ((), ())),
        preferred_element_type=jnp.float32,
    )
    bias = lax.dynamic_slice_in_dim(b_dense, groups * 2 * width, 2 * width).reshape(2, width)
    own_first = jnp.stack([bias[side], bias[1 - side]]).astype(jnp.float32)
    attn = (mixed + own_first).astype(jnp.bfloat16)
    ordered = jnp.where(side == 0, attn, attn[:, :, ::-1])
    own_rows = lax.all_to_all(ordered, ("x", "z"), split_axis=0, concat_axis=0, tiled=True)
    return jnp.transpose(own_rows.reshape(pairs, per_device, 2 * width), (1, 0, 2)).reshape(per_device, -1)


def solution(mesh):
    reps = mesh.shape["rep"]
    coords = [d.coords for d in mesh.devices[0]]
    x_size = len({c[0] for c in coords})
    z_size = len({c[2] for c in coords})
    devices = mesh.devices.reshape(reps, x_size, z_size, -1)
    mesh = jax.sharding.Mesh(devices, ("rep",) + TP)
    placed = (
        P(("rep",) + TP, None),
        P(),
        P(),
        P(None, TP),
        P(TP),
        P(None, TP),
        P(),
        P(None, "rep", None, TP),
        P(None, "rep", None, TP),
        P("rep"),
        P("rep"),
        P("rep"),
        P("rep", None),
    )
    return jax.shard_map(
        on_device, mesh=mesh, in_specs=placed, out_specs=P(("rep",) + TP, None), check_vma=False
    )
```

```python
import math

import jax
import jax.numpy as jnp
from jax import lax
from jax.sharding import PartitionSpec as P

ROT = 24


def layer_norm(rows, gain, shift):
    value_matrix = rows.astype(jnp.float32)
    center = value_matrix - jnp.mean(value_matrix, axis=-1, keepdims=True)
    spread = jnp.mean(center * center, axis=-1, keepdims=True)
    scaled = center * lax.rsqrt(spread + 1e-05)
    return (scaled * gain.astype(jnp.float32) + shift.astype(jnp.float32)).astype(jnp.bfloat16)


def rotary_tables(places, rot_dims):
    counter = jnp.arange(rot_dims // 2, dtype=jnp.float32)
    inverse = jnp.exp(counter * (-2.0 * math.log(10000.0) / rot_dims))
    angles = places.astype(jnp.float32)[:, None] * inverse[None, :]
    return (jnp.cos(angles), jnp.sin(angles))


def rotate(field, cosine, sine):
    half = cosine.shape[-1]
    first = field[..., :half]
    second = field[..., half : 2 * half]
    return jnp.concatenate(
        [first * cosine - second * sine, second * cosine + first * sine, field[..., 2 * half :]],
        axis=-1,
    )


def token_places(span_lens, cache_lens, span_rows):
    within = jnp.arange(span_rows, dtype=jnp.int32)
    prefill = (span_lens[:, None] + within[None, :]).reshape(-1)
    return jnp.concatenate([prefill, cache_lens])


def batch_stacked(form, left, right):
    return jnp.einsum(form, left, right, preferred_element_type=jnp.float32)


def attend(logit_scores, live, value_matrix):
    peaks = jnp.max(jnp.where(live, logit_scores, -1e30), axis=-1, keepdims=True)
    raised = jnp.where(live, jnp.exp(logit_scores - peaks), 0.0)
    softmax_weights = (raised / jnp.sum(raised, axis=-1, keepdims=True)).astype(jnp.bfloat16)
    return batch_stacked("lsw,lwe->lse", softmax_weights, value_matrix).astype(jnp.bfloat16)


def prefill_attention(
    query, keys, value_matrix, prefix_keys, prefix_vals, span_lens, decode_rows, score_scale
):
    spans = prefix_keys.shape[0]
    slots = prefix_keys.shape[1]
    span_rows = (query.shape[0] - decode_rows) // spans
    prefill_rows = spans * span_rows
    head = query.shape[-1]
    prefill_query_span = query[:prefill_rows].reshape(spans, span_rows, head)
    combined_key_rows = jnp.concatenate(
        [prefix_keys, keys[:prefill_rows].reshape(spans, span_rows, head)], axis=1
    )
    all_vals = jnp.concatenate(
        [prefix_vals, value_matrix[:prefill_rows].reshape(spans, span_rows, head)], axis=1
    )
    logit_scores = (
        batch_stacked("jrf,jyf->jry", prefill_query_span, combined_key_rows) * score_scale
    )
    column = jnp.arange(slots + span_rows, dtype=jnp.int32)[None, None, :]
    row_index = jnp.arange(span_rows, dtype=jnp.int32)[None, :, None]
    live = jnp.where(column < slots, column < span_lens[:, None, None], column - slots <= row_index)
    return attend(logit_scores, live, all_vals).reshape(prefill_rows, head)


def decode_attention(
    query, keys, value_matrix, stored_key_cache, cache_vals, cache_lens, slot_valid, score_scale
):
    decode_rows = stored_key_cache.shape[0]
    slots = stored_key_cache.shape[1]
    first_row = query.shape[0] - decode_rows
    decode_query_row = query[first_row:]
    own_keys = keys[first_row:]
    own_vals = value_matrix[first_row:]
    cache_present = (
        batch_stacked("jrf,jyf->jry", decode_query_row[:, None, :], stored_key_cache) * score_scale
    )
    itself = (
        jnp.sum(decode_query_row.astype(jnp.float32) * own_keys.astype(jnp.float32), axis=-1)[
            :, None, None
        ]
        * score_scale
    )
    logit_scores = jnp.concatenate([cache_present, itself], axis=-1)
    column = jnp.arange(slots, dtype=jnp.int32)[None, :]
    live_cache = (column < cache_lens[:, None]) & (slot_valid == 1)
    live = jnp.concatenate([live_cache, jnp.ones((decode_rows, 1), dtype=bool)], axis=-1)[
        :, None, :
    ]
    all_vals = jnp.concatenate([cache_vals, own_vals[:, None, :]], axis=1)
    return attend(logit_scores, live, all_vals)[:, 0, :]


TP = ("x", "z", "yl")


def gather_rows(block):
    pair = lax.all_gather(block, "yl", axis=0, tiled=True)
    return lax.all_gather(pair, ("x", "z"), axis=0, tiled=True)


def ring_stack(block, axis):
    n = lax.axis_size(axis)
    here = lax.axis_index(axis)
    stack = jnp.zeros((n,) + block.shape, block.dtype)
    stack = lax.dynamic_update_index_in_dim(stack, block, here, 0)
    ahead = behind = block
    for step in range(1, n // 2 + 1):
        ahead = lax.ppermute(ahead, axis, [(i, (i + 1) % n) for i in range(n)])
        stack = lax.dynamic_update_index_in_dim(stack, ahead, (here - step) % n, 0)
        if step < n - step:
            behind = lax.ppermute(behind, axis, [(i, (i - 1) % n) for i in range(n)])
            stack = lax.dynamic_update_index_in_dim(stack, behind, (here + step) % n, 0)
    return stack


def layer(
    tokens,
    ln_gain,
    ln_bias,
    w_qkv,
    b_qkv,
    w_dense,
    b_dense,
    prefix_kv,
    decode_kv,
    prefix_lens,
    span_request,
    decode_lens,
    slot_valid,
):
    other_w = lax.ppermute(w_dense, "yl", [(0, 1), (1, 0)])
    normed = layer_norm(tokens, ln_gain, ln_bias)
    joined = jnp.dot(gather_rows(normed), w_qkv, preferred_element_type=jnp.float32)
    joined = joined + b_qkv.astype(jnp.float32)
    head = joined.shape[1] // 3
    token_count = joined.shape[0]
    spans = prefix_kv.shape[1]
    decode_rows = decode_kv.shape[1]
    span_rows = (token_count - decode_rows) // spans
    span_lens = jnp.take(prefix_lens, span_request, axis=0)
    cosine, sine = rotary_tables(token_places(span_lens, decode_lens, span_rows), ROT)
    query = rotate(joined[:, :head], cosine, sine).astype(jnp.bfloat16)
    keys = rotate(joined[:, head : 2 * head], cosine, sine).astype(jnp.bfloat16)
    value_matrix = joined[:, 2 * head :].astype(jnp.bfloat16)
    prefix_keys = jnp.take(prefix_kv[0], span_request, axis=0)
    prefix_vals = jnp.take(prefix_kv[1], span_request, axis=0)
    score_scale = 1.0 / math.sqrt(head)
    early = prefill_attention(
        query, keys, value_matrix, prefix_keys, prefix_vals, span_lens, decode_rows, score_scale
    )
    late = decode_attention(
        query, keys, value_matrix, decode_kv[0], decode_kv[1], decode_lens, slot_valid, score_scale
    )
    heads_out = jnp.concatenate([early, late], axis=0)
    attn = dense_in_pairs(heads_out, w_dense, other_w, b_dense)
    return (attn.astype(jnp.float32) + tokens.astype(jnp.float32)).astype(jnp.bfloat16)


def dense_in_pairs(heads_out, w_dense, other_w, b_dense):
    partner = [(0, 1), (1, 0)]
    side = lax.axis_index("yl")
    rows, head = heads_out.shape
    width = w_dense.shape[1]
    groups = lax.axis_index(("x", "z"))
    per_device = rows // (2 * lax.axis_size(("x", "z")))
    by_owner = heads_out.reshape(-1, 2, per_device, head)
    mine = lax.dynamic_index_in_dim(by_owner, side, axis=1, keepdims=False)
    theirs = lax.dynamic_index_in_dim(by_owner, 1 - side, axis=1, keepdims=False)
    got = lax.ppermute(theirs, "yl", partner)
    pair_heads = jnp.stack([mine, got], axis=1)
    pair_heads = jnp.where(side == 0, pair_heads, pair_heads[:, ::-1])
    every = ring_stack(ring_stack(pair_heads, "z"), "x")
    every = every.reshape((-1,) + pair_heads.shape)
    pairs = every.shape[0]
    w_pair = jnp.stack([w_dense, other_w]).reshape(2, pairs, 2, head, width)
    mixed = lax.dot_general(
        every,
        w_pair,
        (((0, 2, 4), (1, 2, 3)), ((), ())),
        preferred_element_type=jnp.float32,
    )
    bias = lax.dynamic_slice_in_dim(b_dense, groups * 2 * width, 2 * width).reshape(2, width)
    own_first = jnp.stack([bias[side], bias[1 - side]]).astype(jnp.float32)
    attn = (mixed + own_first).astype(jnp.bfloat16)
    ordered = jnp.where(side == 0, attn, attn[:, :, ::-1])
    own_rows = lax.all_to_all(ordered, ("x", "z"), split_axis=0, concat_axis=0, tiled=True)
    return jnp.transpose(own_rows.reshape(pairs, per_device, 2 * width), (1, 0, 2)).reshape(per_device, -1)


def solution(mesh):
    reps = mesh.shape["rep"]
    coords = [d.coords for d in mesh.devices[0]]
    x_size = len({c[0] for c in coords})
    z_size = len({c[2] for c in coords})
    devices = mesh.devices.reshape(reps, x_size, z_size, -1)
    mesh = jax.sharding.Mesh(devices, ("rep",) + TP)
    placed = (
        P(("rep",) + TP, None),
        P(),
        P(),
        P(None, TP),
        P(TP),
        P(None, TP),
        P(),
        P(None, "rep", None, TP),
        P(None, "rep", None, TP),
        P("rep"),
        P("rep"),
        P("rep"),
        P("rep", None),
    )
    return jax.shard_map(
        layer, mesh=mesh, in_specs=placed, out_specs=P(("rep",) + TP, None), check_vma=False
    )
```

```python
import math

import jax
import jax.numpy as jnp
from jax import lax
from jax.sharding import PartitionSpec as P

ROT = 24


def layer_norm(rows, gain, shift):
    value_matrix = rows.astype(jnp.float32)
    center = value_matrix - jnp.mean(value_matrix, axis=-1, keepdims=True)
    spread = jnp.mean(center * center, axis=-1, keepdims=True)
    scaled = center * lax.rsqrt(spread + 1e-05)
    return (scaled * gain.astype(jnp.float32) + shift.astype(jnp.float32)).astype(jnp.bfloat16)


def rotary_tables(places, rot_dims):
    counter = jnp.arange(rot_dims // 2, dtype=jnp.float32)
    inverse = jnp.exp(counter * (-2.0 * math.log(10000.0) / rot_dims))
    angles = places.astype(jnp.float32)[:, None] * inverse[None, :]
    return (jnp.cos(angles), jnp.sin(angles))


def rotate(field, cosine, sine):
    half = cosine.shape[-1]
    first = field[..., :half]
    second = field[..., half : 2 * half]
    return jnp.concatenate(
        [first * cosine - second * sine, second * cosine + first * sine, field[..., 2 * half :]],
        axis=-1,
    )


def token_places(span_lens, cache_lens, span_rows):
    within = jnp.arange(span_rows, dtype=jnp.int32)
    prefill = (span_lens[:, None] + within[None, :]).reshape(-1)
    return jnp.concatenate([prefill, cache_lens])


def batch_stacked(form, left, right):
    return jnp.einsum(form, left, right, preferred_element_type=jnp.float32)


def attend(logit_scores, live, value_matrix):
    peaks = jnp.max(jnp.where(live, logit_scores, -1e30), axis=-1, keepdims=True)
    raised = jnp.where(live, jnp.exp(logit_scores - peaks), 0.0)
    softmax_weights = (raised / jnp.sum(raised, axis=-1, keepdims=True)).astype(jnp.bfloat16)
    return batch_stacked("lsw,lwe->lse", softmax_weights, value_matrix).astype(jnp.bfloat16)


def prefill_attention(
    query, keys, value_matrix, prefix_keys, prefix_vals, span_lens, decode_rows, score_scale
):
    spans = prefix_keys.shape[0]
    slots = prefix_keys.shape[1]
    span_rows = (query.shape[0] - decode_rows) // spans
    prefill_rows = spans * span_rows
    head = query.shape[-1]
    prefill_query_span = query[:prefill_rows].reshape(spans, span_rows, head)
    combined_key_rows = jnp.concatenate(
        [prefix_keys, keys[:prefill_rows].reshape(spans, span_rows, head)], axis=1
    )
    all_vals = jnp.concatenate(
        [prefix_vals, value_matrix[:prefill_rows].reshape(spans, span_rows, head)], axis=1
    )
    logit_scores = (
        batch_stacked("jrf,jyf->jry", prefill_query_span, combined_key_rows) * score_scale
    )
    column = jnp.arange(slots + span_rows, dtype=jnp.int32)[None, None, :]
    row_index = jnp.arange(span_rows, dtype=jnp.int32)[None, :, None]
    live = jnp.where(column < slots, column < span_lens[:, None, None], column - slots <= row_index)
    return attend(logit_scores, live, all_vals).reshape(prefill_rows, head)


def decode_attention(
    query, keys, value_matrix, stored_key_cache, cache_vals, cache_lens, slot_valid, score_scale
):
    decode_rows = stored_key_cache.shape[0]
    slots = stored_key_cache.shape[1]
    first_row = query.shape[0] - decode_rows
    decode_query_row = query[first_row:]
    own_keys = keys[first_row:]
    own_vals = value_matrix[first_row:]
    cache_present = (
        batch_stacked("jrf,jyf->jry", decode_query_row[:, None, :], stored_key_cache) * score_scale
    )
    itself = (
        jnp.sum(decode_query_row.astype(jnp.float32) * own_keys.astype(jnp.float32), axis=-1)[
            :, None, None
        ]
        * score_scale
    )
    logit_scores = jnp.concatenate([cache_present, itself], axis=-1)
    column = jnp.arange(slots, dtype=jnp.int32)[None, :]
    live_cache = (column < cache_lens[:, None]) & (slot_valid == 1)
    live = jnp.concatenate([live_cache, jnp.ones((decode_rows, 1), dtype=bool)], axis=-1)[
        :, None, :
    ]
    all_vals = jnp.concatenate([cache_vals, own_vals[:, None, :]], axis=1)
    return attend(logit_scores, live, all_vals)[:, 0, :]


TP = ("x", "z", "yl")


def gather_rows(block):
    pair = lax.all_gather(block, "yl", axis=0, tiled=True)
    return lax.all_gather(pair, ("x", "z"), axis=0, tiled=True)


def layer(
    tokens,
    ln_gain,
    ln_bias,
    w_qkv,
    b_qkv,
    w_dense,
    b_dense,
    prefix_kv,
    decode_kv,
    prefix_lens,
    span_request,
    decode_lens,
    slot_valid,
):
    other_w = lax.ppermute(w_dense, "yl", [(0, 1), (1, 0)])
    normed = layer_norm(tokens, ln_gain, ln_bias)
    joined = jnp.dot(gather_rows(normed), w_qkv, preferred_element_type=jnp.float32)
    joined = joined + b_qkv.astype(jnp.float32)
    head = joined.shape[1] // 3
    token_count = joined.shape[0]
    spans = prefix_kv.shape[1]
    decode_rows = decode_kv.shape[1]
    span_rows = (token_count - decode_rows) // spans
    span_lens = jnp.take(prefix_lens, span_request, axis=0)
    cosine, sine = rotary_tables(token_places(span_lens, decode_lens, span_rows), ROT)
    query = rotate(joined[:, :head], cosine, sine).astype(jnp.bfloat16)
    keys = rotate(joined[:, head : 2 * head], cosine, sine).astype(jnp.bfloat16)
    value_matrix = joined[:, 2 * head :].astype(jnp.bfloat16)
    prefix_keys = jnp.take(prefix_kv[0], span_request, axis=0)
    prefix_vals = jnp.take(prefix_kv[1], span_request, axis=0)
    score_scale = 1.0 / math.sqrt(head)
    early = prefill_attention(
        query, keys, value_matrix, prefix_keys, prefix_vals, span_lens, decode_rows, score_scale
    )
    late = decode_attention(
        query, keys, value_matrix, decode_kv[0], decode_kv[1], decode_lens, slot_valid, score_scale
    )
    heads_out = jnp.concatenate([early, late], axis=0)
    attn = dense_in_pairs(heads_out, w_dense, other_w, b_dense)
    return (attn.astype(jnp.float32) + tokens.astype(jnp.float32)).astype(jnp.bfloat16)


def dense_in_pairs(heads_out, w_dense, other_w, b_dense):
    partner = [(0, 1), (1, 0)]
    side = lax.axis_index("yl")
    rows, head = heads_out.shape
    width = w_dense.shape[1]
    groups = lax.axis_index(("x", "z"))
    per_device = rows // (2 * lax.axis_size(("x", "z")))
    by_owner = heads_out.reshape(-1, 2, per_device, head)
    mine = lax.dynamic_index_in_dim(by_owner, side, axis=1, keepdims=False)
    theirs = lax.dynamic_index_in_dim(by_owner, 1 - side, axis=1, keepdims=False)
    got = lax.ppermute(theirs, "yl", partner)
    pair_heads = jnp.stack([mine, got], axis=1)
    pair_heads = jnp.where(side == 0, pair_heads, pair_heads[:, ::-1])
    along_z = lax.all_gather(pair_heads, "z", axis=0, tiled=False)
    every = lax.all_gather(along_z, "x", axis=0, tiled=False)
    every = every.reshape((-1,) + pair_heads.shape)
    pairs = every.shape[0]
    w_pair = jnp.stack([w_dense, other_w]).reshape(2, pairs, 2, head, width)
    mixed = lax.dot_general(
        every,
        w_pair,
        (((0, 2, 4), (1, 2, 3)), ((), ())),
        preferred_element_type=jnp.float32,
    )
    bias = lax.dynamic_slice_in_dim(b_dense, groups * 2 * width, 2 * width).reshape(2, width)
    own_first = jnp.stack([bias[side], bias[1 - side]]).astype(jnp.float32)
    attn = (mixed + own_first).astype(jnp.bfloat16)
    ordered = jnp.where(side == 0, attn, attn[:, :, ::-1])
    own_rows = lax.all_to_all(ordered, ("x", "z"), split_axis=0, concat_axis=0, tiled=True)
    return jnp.transpose(own_rows.reshape(pairs, per_device, 2 * width), (1, 0, 2)).reshape(per_device, -1)


def solution(mesh):
    reps = mesh.shape["rep"]
    coords = [d.coords for d in mesh.devices[0]]
    x_size = len({c[0] for c in coords})
    z_size = len({c[2] for c in coords})
    devices = mesh.devices.reshape(reps, x_size, z_size, -1)
    mesh = jax.sharding.Mesh(devices, ("rep",) + TP)
    placed = (
        P(("rep",) + TP, None),
        P(),
        P(),
        P(None, TP),
        P(TP),
        P(None, TP),
        P(),
        P(None, "rep", None, TP),
        P(None, "rep", None, TP),
        P("rep"),
        P("rep"),
        P("rep"),
        P("rep", None),
    )
    return jax.shard_map(
        layer, mesh=mesh, in_specs=placed, out_specs=P(("rep",) + TP, None), check_vma=False
    )
```

```python
import math

import jax
import jax.numpy as jnp
from jax import lax
from jax.sharding import PartitionSpec as P

ROT = 24


def layer_norm(rows, gain, shift):
    value_matrix = rows.astype(jnp.float32)
    center = value_matrix - jnp.mean(value_matrix, axis=-1, keepdims=True)
    spread = jnp.mean(center * center, axis=-1, keepdims=True)
    scaled = center * lax.rsqrt(spread + 1e-05)
    return (scaled * gain.astype(jnp.float32) + shift.astype(jnp.float32)).astype(jnp.bfloat16)


def rotary_tables(places, rot_dims):
    counter = jnp.arange(rot_dims // 2, dtype=jnp.float32)
    inverse = jnp.exp(counter * (-2.0 * math.log(10000.0) / rot_dims))
    angles = places.astype(jnp.float32)[:, None] * inverse[None, :]
    return (jnp.cos(angles), jnp.sin(angles))


def rotate(field, cosine, sine):
    half = cosine.shape[-1]
    first = field[..., :half]
    second = field[..., half : 2 * half]
    return jnp.concatenate(
        [first * cosine - second * sine, second * cosine + first * sine, field[..., 2 * half :]],
        axis=-1,
    )


def token_places(span_lens, cache_lens, span_rows):
    within = jnp.arange(span_rows, dtype=jnp.int32)
    prefill = (span_lens[:, None] + within[None, :]).reshape(-1)
    return jnp.concatenate([prefill, cache_lens])


def batch_stacked(form, left, right):
    return jnp.einsum(form, left, right, preferred_element_type=jnp.float32)


def attend(logit_scores, live, value_matrix):
    peaks = jnp.max(jnp.where(live, logit_scores, -1e30), axis=-1, keepdims=True)
    raised = jnp.where(live, jnp.exp(logit_scores - peaks), 0.0)
    softmax_weights = (raised / jnp.sum(raised, axis=-1, keepdims=True)).astype(jnp.bfloat16)
    return batch_stacked("lsw,lwe->lse", softmax_weights, value_matrix).astype(jnp.bfloat16)


def prefill_attention(
    query, keys, value_matrix, prefix_keys, prefix_vals, span_lens, decode_rows, score_scale
):
    spans = prefix_keys.shape[0]
    slots = prefix_keys.shape[1]
    span_rows = (query.shape[0] - decode_rows) // spans
    prefill_rows = spans * span_rows
    head = query.shape[-1]
    prefill_query_span = query[:prefill_rows].reshape(spans, span_rows, head)
    combined_key_rows = jnp.concatenate(
        [prefix_keys, keys[:prefill_rows].reshape(spans, span_rows, head)], axis=1
    )
    all_vals = jnp.concatenate(
        [prefix_vals, value_matrix[:prefill_rows].reshape(spans, span_rows, head)], axis=1
    )
    logit_scores = (
        batch_stacked("jrf,jyf->jry", prefill_query_span, combined_key_rows) * score_scale
    )
    column = jnp.arange(slots + span_rows, dtype=jnp.int32)[None, None, :]
    row_index = jnp.arange(span_rows, dtype=jnp.int32)[None, :, None]
    live = jnp.where(column < slots, column < span_lens[:, None, None], column - slots <= row_index)
    return attend(logit_scores, live, all_vals).reshape(prefill_rows, head)


def decode_attention(
    query, keys, value_matrix, stored_key_cache, cache_vals, cache_lens, slot_valid, score_scale
):
    decode_rows = stored_key_cache.shape[0]
    slots = stored_key_cache.shape[1]
    first_row = query.shape[0] - decode_rows
    decode_query_row = query[first_row:]
    own_keys = keys[first_row:]
    own_vals = value_matrix[first_row:]
    cache_present = (
        batch_stacked("jrf,jyf->jry", decode_query_row[:, None, :], stored_key_cache) * score_scale
    )
    itself = (
        jnp.sum(decode_query_row.astype(jnp.float32) * own_keys.astype(jnp.float32), axis=-1)[
            :, None, None
        ]
        * score_scale
    )
    logit_scores = jnp.concatenate([cache_present, itself], axis=-1)
    column = jnp.arange(slots, dtype=jnp.int32)[None, :]
    live_cache = (column < cache_lens[:, None]) & (slot_valid == 1)
    live = jnp.concatenate([live_cache, jnp.ones((decode_rows, 1), dtype=bool)], axis=-1)[
        :, None, :
    ]
    all_vals = jnp.concatenate([cache_vals, own_vals[:, None, :]], axis=1)
    return attend(logit_scores, live, all_vals)[:, 0, :]


TP = ("x", "z", "yl")


def gather_rows(block):
    pair = lax.all_gather(block, "yl", axis=0, tiled=True)
    return lax.all_gather(pair, ("x", "z"), axis=0, tiled=True)


def gather_heads(block):
    pair = lax.all_gather(block, "yl", axis=0, tiled=False)
    every = lax.all_gather(pair, ("x", "z"), axis=0, tiled=False)
    return every.reshape((-1,) + block.shape)


def on_device(
    tokens,
    ln_gain,
    ln_bias,
    w_qkv,
    b_qkv,
    w_dense,
    b_dense,
    prefix_kv,
    decode_kv,
    prefix_lens,
    span_request,
    decode_lens,
    slot_valid,
):
    normed = layer_norm(tokens, ln_gain, ln_bias)
    joined = jnp.dot(gather_rows(normed), w_qkv, preferred_element_type=jnp.float32)
    joined = joined + b_qkv.astype(jnp.float32)
    head = joined.shape[1] // 3
    token_count = joined.shape[0]
    spans = prefix_kv.shape[1]
    decode_rows = decode_kv.shape[1]
    span_rows = (token_count - decode_rows) // spans
    span_lens = jnp.take(prefix_lens, span_request, axis=0)
    cosine, sine = rotary_tables(token_places(span_lens, decode_lens, span_rows), ROT)
    query = rotate(joined[:, :head], cosine, sine).astype(jnp.bfloat16)
    keys = rotate(joined[:, head : 2 * head], cosine, sine).astype(jnp.bfloat16)
    value_matrix = joined[:, 2 * head :].astype(jnp.bfloat16)
    prefix_keys = jnp.take(prefix_kv[0], span_request, axis=0)
    prefix_vals = jnp.take(prefix_kv[1], span_request, axis=0)
    score_scale = 1.0 / math.sqrt(head)
    early = prefill_attention(
        query, keys, value_matrix, prefix_keys, prefix_vals, span_lens, decode_rows, score_scale
    )
    late = decode_attention(
        query, keys, value_matrix, decode_kv[0], decode_kv[1], decode_lens, slot_valid, score_scale
    )
    heads_out = jnp.concatenate([early, late], axis=0)
    attn = dense_in_pairs(heads_out, w_dense, b_dense)
    return (attn.astype(jnp.float32) + tokens.astype(jnp.float32)).astype(jnp.bfloat16)


def dense_in_pairs(heads_out, w_dense, b_dense):
    partner = [(0, 1), (1, 0)]
    side = lax.axis_index("yl")
    rows, head = heads_out.shape
    width = w_dense.shape[1]
    groups = lax.axis_index(("x", "z"))
    per_device = rows // (2 * lax.axis_size(("x", "z")))
    other_w = lax.ppermute(w_dense, "yl", partner)
    by_owner = heads_out.reshape(-1, 2, per_device, head)
    mine = lax.dynamic_index_in_dim(by_owner, side, axis=1, keepdims=False)
    theirs = lax.dynamic_index_in_dim(by_owner, 1 - side, axis=1, keepdims=False)
    got = lax.ppermute(theirs, "yl", partner)
    pair_heads = jnp.stack([mine, got], axis=1)
    pair_heads = jnp.where(side == 0, pair_heads, pair_heads[:, ::-1])
    every = lax.all_gather(pair_heads, ("x", "z"), axis=0, tiled=False)
    pairs = every.shape[0]
    w_pair = jnp.stack([w_dense, other_w]).reshape(2, pairs, 2, head, width)
    mixed = lax.dot_general(
        every,
        w_pair,
        (((0, 2, 4), (1, 2, 3)), ((), ())),
        preferred_element_type=jnp.float32,
    )
    bias = lax.dynamic_slice_in_dim(b_dense, groups * 2 * width, 2 * width).reshape(2, width)
    own_first = jnp.stack([bias[side], bias[1 - side]]).astype(jnp.float32)
    attn = (mixed + own_first).astype(jnp.bfloat16)
    ordered = jnp.where(side == 0, attn, attn[:, :, ::-1])
    ordered = ordered.reshape(pairs, per_device, 1, 2 * width)
    own_rows = lax.all_to_all(ordered, ("x", "z"), split_axis=0, concat_axis=2, tiled=True)
    return own_rows.reshape(per_device, -1)


def solution(mesh):
    reps = mesh.shape["rep"]
    coords = [d.coords for d in mesh.devices[0]]
    x_size = len({c[0] for c in coords})
    z_size = len({c[2] for c in coords})
    devices = mesh.devices.reshape(reps, x_size, z_size, -1)
    mesh = jax.sharding.Mesh(devices, ("rep",) + TP)
    placed = (
        P(("rep",) + TP, None),
        P(),
        P(),
        P(None, TP),
        P(TP),
        P(None, TP),
        P(),
        P(None, "rep", None, TP),
        P(None, "rep", None, TP),
        P("rep"),
        P("rep"),
        P("rep"),
        P("rep", None),
    )
    return jax.shard_map(
        on_device, mesh=mesh, in_specs=placed, out_specs=P(("rep",) + TP, None), check_vma=False
    )
```

```python
import math

import jax
import jax.numpy as jnp
from jax import lax
from jax.sharding import PartitionSpec as P

ROT = 24


def layer_norm(rows, gain, shift):
    value_matrix = rows.astype(jnp.float32)
    center = value_matrix - jnp.mean(value_matrix, axis=-1, keepdims=True)
    spread = jnp.mean(center * center, axis=-1, keepdims=True)
    scaled = center * lax.rsqrt(spread + 1e-05)
    return (scaled * gain.astype(jnp.float32) + shift.astype(jnp.float32)).astype(jnp.bfloat16)


def rotary_tables(places, rot_dims):
    counter = jnp.arange(rot_dims // 2, dtype=jnp.float32)
    inverse = jnp.exp(counter * (-2.0 * math.log(10000.0) / rot_dims))
    angles = places.astype(jnp.float32)[:, None] * inverse[None, :]
    return (jnp.cos(angles), jnp.sin(angles))


def rotate(field, cosine, sine):
    half = cosine.shape[-1]
    first = field[..., :half]
    second = field[..., half : 2 * half]
    return jnp.concatenate(
        [first * cosine - second * sine, second * cosine + first * sine, field[..., 2 * half :]],
        axis=-1,
    )


def token_places(span_lens, cache_lens, span_rows):
    within = jnp.arange(span_rows, dtype=jnp.int32)
    prefill = (span_lens[:, None] + within[None, :]).reshape(-1)
    return jnp.concatenate([prefill, cache_lens])


def batch_stacked(form, left, right):
    return jnp.einsum(form, left, right, preferred_element_type=jnp.float32)


def attend(logit_scores, live, value_matrix):
    peaks = jnp.max(jnp.where(live, logit_scores, -1e30), axis=-1, keepdims=True)
    raised = jnp.where(live, jnp.exp(logit_scores - peaks), 0.0)
    softmax_weights = (raised / jnp.sum(raised, axis=-1, keepdims=True)).astype(jnp.bfloat16)
    return batch_stacked("lsw,lwe->lse", softmax_weights, value_matrix).astype(jnp.bfloat16)


def prefill_attention(
    query, keys, value_matrix, prefix_keys, prefix_vals, span_lens, decode_rows, score_scale
):
    spans = prefix_keys.shape[0]
    slots = prefix_keys.shape[1]
    span_rows = (query.shape[0] - decode_rows) // spans
    prefill_rows = spans * span_rows
    head = query.shape[-1]
    prefill_query_span = query[:prefill_rows].reshape(spans, span_rows, head)
    combined_key_rows = jnp.concatenate(
        [prefix_keys, keys[:prefill_rows].reshape(spans, span_rows, head)], axis=1
    )
    all_vals = jnp.concatenate(
        [prefix_vals, value_matrix[:prefill_rows].reshape(spans, span_rows, head)], axis=1
    )
    logit_scores = (
        batch_stacked("jrf,jyf->jry", prefill_query_span, combined_key_rows) * score_scale
    )
    column = jnp.arange(slots + span_rows, dtype=jnp.int32)[None, None, :]
    row_index = jnp.arange(span_rows, dtype=jnp.int32)[None, :, None]
    live = jnp.where(column < slots, column < span_lens[:, None, None], column - slots <= row_index)
    return attend(logit_scores, live, all_vals).reshape(prefill_rows, head)


def decode_attention(
    query, keys, value_matrix, stored_key_cache, cache_vals, cache_lens, slot_valid, score_scale
):
    decode_rows = stored_key_cache.shape[0]
    slots = stored_key_cache.shape[1]
    first_row = query.shape[0] - decode_rows
    decode_query_row = query[first_row:]
    own_keys = keys[first_row:]
    own_vals = value_matrix[first_row:]
    cache_present = (
        batch_stacked("jrf,jyf->jry", decode_query_row[:, None, :], stored_key_cache) * score_scale
    )
    itself = (
        jnp.sum(decode_query_row.astype(jnp.float32) * own_keys.astype(jnp.float32), axis=-1)[
            :, None, None
        ]
        * score_scale
    )
    logit_scores = jnp.concatenate([cache_present, itself], axis=-1)
    column = jnp.arange(slots, dtype=jnp.int32)[None, :]
    live_cache = (column < cache_lens[:, None]) & (slot_valid == 1)
    live = jnp.concatenate([live_cache, jnp.ones((decode_rows, 1), dtype=bool)], axis=-1)[
        :, None, :
    ]
    all_vals = jnp.concatenate([cache_vals, own_vals[:, None, :]], axis=1)
    return attend(logit_scores, live, all_vals)[:, 0, :]


TP = ("x", "z", "yl")


def gather_rows(block):
    pair = lax.all_gather(block, "yl", axis=0, tiled=True)
    return lax.all_gather(pair, ("x", "z"), axis=0, tiled=True)


def gather_heads(block):
    pair = lax.all_gather(block, "yl", axis=0, tiled=False)
    every = lax.all_gather(pair, ("x", "z"), axis=0, tiled=False)
    return every.reshape((-1,) + block.shape)


def on_device(
    tokens,
    ln_gain,
    ln_bias,
    w_qkv,
    b_qkv,
    w_dense,
    b_dense,
    prefix_kv,
    decode_kv,
    prefix_lens,
    span_request,
    decode_lens,
    slot_valid,
):
    normed = layer_norm(tokens, ln_gain, ln_bias)
    joined = jnp.dot(gather_rows(normed), w_qkv, preferred_element_type=jnp.float32)
    joined = joined + b_qkv.astype(jnp.float32)
    head = joined.shape[1] // 3
    token_count = joined.shape[0]
    spans = prefix_kv.shape[1]
    decode_rows = decode_kv.shape[1]
    span_rows = (token_count - decode_rows) // spans
    span_lens = jnp.take(prefix_lens, span_request, axis=0)
    cosine, sine = rotary_tables(token_places(span_lens, decode_lens, span_rows), ROT)
    query = rotate(joined[:, :head], cosine, sine).astype(jnp.bfloat16)
    keys = rotate(joined[:, head : 2 * head], cosine, sine).astype(jnp.bfloat16)
    value_matrix = joined[:, 2 * head :].astype(jnp.bfloat16)
    prefix_keys = jnp.take(prefix_kv[0], span_request, axis=0)
    prefix_vals = jnp.take(prefix_kv[1], span_request, axis=0)
    score_scale = 1.0 / math.sqrt(head)
    early = prefill_attention(
        query, keys, value_matrix, prefix_keys, prefix_vals, span_lens, decode_rows, score_scale
    )
    late = decode_attention(
        query, keys, value_matrix, decode_kv[0], decode_kv[1], decode_lens, slot_valid, score_scale
    )
    heads_out = jnp.concatenate([early, late], axis=0)
    attn = dense_in_pairs(heads_out, w_dense, b_dense)
    return (attn.astype(jnp.float32) + tokens.astype(jnp.float32)).astype(jnp.bfloat16)


def dense_in_pairs(heads_out, w_dense, b_dense):
    partner = [(0, 1), (1, 0)]
    side = lax.axis_index("yl")
    rows, head = heads_out.shape
    width = w_dense.shape[1]
    groups = lax.axis_index(("x", "z"))
    per_device = rows // (2 * lax.axis_size(("x", "z")))
    other_w = lax.ppermute(w_dense, "yl", partner)
    by_owner = heads_out.reshape(-1, 2, per_device, head)
    mine = lax.dynamic_index_in_dim(by_owner, side, axis=1, keepdims=False)
    theirs = lax.dynamic_index_in_dim(by_owner, 1 - side, axis=1, keepdims=False)
    got = lax.ppermute(theirs, "yl", partner)
    pair_heads = jnp.stack([mine, got], axis=1)
    pair_heads = jnp.where(side == 0, pair_heads, pair_heads[:, ::-1])
    along_z = lax.all_gather(pair_heads, "z", axis=0, tiled=False)
    every = lax.all_gather(along_z, "x", axis=0, tiled=False)
    every = every.reshape((-1,) + pair_heads.shape)
    pairs = every.shape[0]
    w_pair = jnp.stack([w_dense, other_w]).reshape(2, pairs, 2, head, width)
    mixed = lax.dot_general(
        every,
        w_pair,
        (((0, 2, 4), (1, 2, 3)), ((), ())),
        preferred_element_type=jnp.float32,
    )
    bias = lax.dynamic_slice_in_dim(b_dense, groups * 2 * width, 2 * width).reshape(2, width)
    own_first = jnp.stack([bias[side], bias[1 - side]]).astype(jnp.float32)
    attn = (mixed + own_first).astype(jnp.bfloat16)
    ordered = jnp.where(side == 0, attn, attn[:, :, ::-1])
    ordered = ordered.reshape(pairs, per_device, 1, 2 * width)
    own_rows = lax.all_to_all(ordered, ("x", "z"), split_axis=0, concat_axis=2, tiled=True)
    return own_rows.reshape(per_device, -1)


def solution(mesh):
    reps = mesh.shape["rep"]
    coords = [d.coords for d in mesh.devices[0]]
    x_size = len({c[0] for c in coords})
    z_size = len({c[2] for c in coords})
    devices = mesh.devices.reshape(reps, x_size, z_size, -1)
    mesh = jax.sharding.Mesh(devices, ("rep",) + TP)
    placed = (
        P(("rep",) + TP, None),
        P(),
        P(),
        P(None, TP),
        P(TP),
        P(None, TP),
        P(),
        P(None, "rep", None, TP),
        P(None, "rep", None, TP),
        P("rep"),
        P("rep"),
        P("rep"),
        P("rep", None),
    )
    return jax.shard_map(
        on_device, mesh=mesh, in_specs=placed, out_specs=P(("rep",) + TP, None), check_vma=False
    )
```

```python
import math

import jax
import jax.numpy as jnp
from jax import lax
from jax.sharding import PartitionSpec as P

ROT = 24


def layer_norm(rows, gain, shift):
    value_matrix = rows.astype(jnp.float32)
    center = value_matrix - jnp.mean(value_matrix, axis=-1, keepdims=True)
    spread = jnp.mean(center * center, axis=-1, keepdims=True)
    scaled = center * lax.rsqrt(spread + 1e-05)
    return (scaled * gain.astype(jnp.float32) + shift.astype(jnp.float32)).astype(jnp.bfloat16)


def rotary_tables(places, rot_dims):
    counter = jnp.arange(rot_dims // 2, dtype=jnp.float32)
    inverse = jnp.exp(counter * (-2.0 * math.log(10000.0) / rot_dims))
    angles = places.astype(jnp.float32)[:, None] * inverse[None, :]
    return (jnp.cos(angles), jnp.sin(angles))


def rotate(field, cosine, sine):
    half = cosine.shape[-1]
    first = field[..., :half]
    second = field[..., half : 2 * half]
    return jnp.concatenate(
        [first * cosine - second * sine, second * cosine + first * sine, field[..., 2 * half :]],
        axis=-1,
    )


def token_places(span_lens, cache_lens, span_rows):
    within = jnp.arange(span_rows, dtype=jnp.int32)
    prefill = (span_lens[:, None] + within[None, :]).reshape(-1)
    return jnp.concatenate([prefill, cache_lens])


def batch_stacked(form, left, right):
    return jnp.einsum(form, left, right, preferred_element_type=jnp.float32)


def attend(logit_scores, live, value_matrix):
    peaks = jnp.max(jnp.where(live, logit_scores, -1e30), axis=-1, keepdims=True)
    raised = jnp.where(live, jnp.exp(logit_scores - peaks), 0.0)
    softmax_weights = (raised / jnp.sum(raised, axis=-1, keepdims=True)).astype(jnp.bfloat16)
    return batch_stacked("lsw,lwe->lse", softmax_weights, value_matrix).astype(jnp.bfloat16)


def prefill_attention(
    query, keys, value_matrix, prefix_keys, prefix_vals, span_lens, decode_rows, score_scale
):
    spans = prefix_keys.shape[0]
    slots = prefix_keys.shape[1]
    span_rows = (query.shape[0] - decode_rows) // spans
    prefill_rows = spans * span_rows
    head = query.shape[-1]
    prefill_query_span = query[:prefill_rows].reshape(spans, span_rows, head)
    combined_key_rows = jnp.concatenate(
        [prefix_keys, keys[:prefill_rows].reshape(spans, span_rows, head)], axis=1
    )
    all_vals = jnp.concatenate(
        [prefix_vals, value_matrix[:prefill_rows].reshape(spans, span_rows, head)], axis=1
    )
    logit_scores = (
        batch_stacked("jrf,jyf->jry", prefill_query_span, combined_key_rows) * score_scale
    )
    column = jnp.arange(slots + span_rows, dtype=jnp.int32)[None, None, :]
    row_index = jnp.arange(span_rows, dtype=jnp.int32)[None, :, None]
    live = jnp.where(column < slots, column < span_lens[:, None, None], column - slots <= row_index)
    return attend(logit_scores, live, all_vals).reshape(prefill_rows, head)


def decode_attention(
    query, keys, value_matrix, stored_key_cache, cache_vals, cache_lens, slot_valid, score_scale
):
    decode_rows = stored_key_cache.shape[0]
    slots = stored_key_cache.shape[1]
    first_row = query.shape[0] - decode_rows
    decode_query_row = query[first_row:]
    own_keys = keys[first_row:]
    own_vals = value_matrix[first_row:]
    cache_present = (
        batch_stacked("jrf,jyf->jry", decode_query_row[:, None, :], stored_key_cache) * score_scale
    )
    itself = (
        jnp.sum(decode_query_row.astype(jnp.float32) * own_keys.astype(jnp.float32), axis=-1)[
            :, None, None
        ]
        * score_scale
    )
    logit_scores = jnp.concatenate([cache_present, itself], axis=-1)
    column = jnp.arange(slots, dtype=jnp.int32)[None, :]
    live_cache = (column < cache_lens[:, None]) & (slot_valid == 1)
    live = jnp.concatenate([live_cache, jnp.ones((decode_rows, 1), dtype=bool)], axis=-1)[
        :, None, :
    ]
    all_vals = jnp.concatenate([cache_vals, own_vals[:, None, :]], axis=1)
    return attend(logit_scores, live, all_vals)[:, 0, :]


TP = ("x", "z", "yl")


def gather_rows(block):
    pair = lax.all_gather(block, "yl", axis=0, tiled=True)
    return lax.all_gather(pair, ("x", "z"), axis=0, tiled=True)


def layer(
    tokens,
    ln_gain,
    ln_bias,
    w_qkv,
    b_qkv,
    w_dense,
    b_dense,
    prefix_kv,
    decode_kv,
    prefix_lens,
    span_request,
    decode_lens,
    slot_valid,
):
    other_w = lax.ppermute(w_dense, "yl", [(0, 1), (1, 0)])
    normed = layer_norm(tokens, ln_gain, ln_bias)
    joined = jnp.dot(gather_rows(normed), w_qkv, preferred_element_type=jnp.float32)
    joined = joined + b_qkv.astype(jnp.float32)
    head = joined.shape[1] // 3
    token_count = joined.shape[0]
    spans = prefix_kv.shape[1]
    decode_rows = decode_kv.shape[1]
    span_rows = (token_count - decode_rows) // spans
    span_lens = jnp.take(prefix_lens, span_request, axis=0)
    cosine, sine = rotary_tables(token_places(span_lens, decode_lens, span_rows), ROT)
    query = rotate(joined[:, :head], cosine, sine).astype(jnp.bfloat16)
    keys = rotate(joined[:, head : 2 * head], cosine, sine).astype(jnp.bfloat16)
    value_matrix = joined[:, 2 * head :].astype(jnp.bfloat16)
    prefix_keys = jnp.take(prefix_kv[0], span_request, axis=0)
    prefix_vals = jnp.take(prefix_kv[1], span_request, axis=0)
    score_scale = 1.0 / math.sqrt(head)
    early = prefill_attention(
        query, keys, value_matrix, prefix_keys, prefix_vals, span_lens, decode_rows, score_scale
    )
    late = decode_attention(
        query, keys, value_matrix, decode_kv[0], decode_kv[1], decode_lens, slot_valid, score_scale
    )
    heads_out = jnp.concatenate([early, late], axis=0)
    attn = dense_in_pairs(heads_out, w_dense, other_w, b_dense)
    return (attn.astype(jnp.float32) + tokens.astype(jnp.float32)).astype(jnp.bfloat16)


def dense_in_pairs(heads_out, w_dense, other_w, b_dense):
    partner = [(0, 1), (1, 0)]
    side = lax.axis_index("yl")
    rows, head = heads_out.shape
    width = w_dense.shape[1]
    groups = lax.axis_index(("x", "z"))
    per_device = rows // (2 * lax.axis_size(("x", "z")))
    by_owner = heads_out.reshape(-1, 2, per_device, head)
    mine = lax.dynamic_index_in_dim(by_owner, side, axis=1, keepdims=False)
    theirs = lax.dynamic_index_in_dim(by_owner, 1 - side, axis=1, keepdims=False)
    got = lax.ppermute(theirs, "yl", partner)
    pair_heads = jnp.stack([mine, got], axis=1)
    pair_heads = jnp.where(side == 0, pair_heads, pair_heads[:, ::-1])
    along_z = lax.all_gather(pair_heads, "z", axis=0, tiled=False)
    every = lax.all_gather(along_z, "x", axis=0, tiled=False)
    every = every.reshape((-1,) + pair_heads.shape)
    pairs = every.shape[0]
    w_pair = jnp.stack([w_dense, other_w]).reshape(2, pairs, 2, head, width)
    mixed = lax.dot_general(
        every,
        w_pair,
        (((0, 2, 4), (1, 2, 3)), ((), ())),
        preferred_element_type=jnp.float32,
    )
    bias = lax.dynamic_slice_in_dim(b_dense, groups * 2 * width, 2 * width).reshape(2, width)
    own_first = jnp.stack([bias[side], bias[1 - side]]).astype(jnp.float32)
    attn = (mixed + own_first).astype(jnp.bfloat16)
    ordered = jnp.where(side == 0, attn, attn[:, :, ::-1])
    ordered = ordered.reshape(pairs, per_device, 1, 2 * width)
    own_rows = lax.all_to_all(ordered, ("x", "z"), split_axis=0, concat_axis=2, tiled=True)
    return own_rows.reshape(per_device, -1)


def solution(mesh):
    reps = mesh.shape["rep"]
    coords = [d.coords for d in mesh.devices[0]]
    x_size = len({c[0] for c in coords})
    z_size = len({c[2] for c in coords})
    devices = mesh.devices.reshape(reps, x_size, z_size, -1)
    mesh = jax.sharding.Mesh(devices, ("rep",) + TP)
    placed = (
        P(("rep",) + TP, None),
        P(),
        P(),
        P(None, TP),
        P(TP),
        P(None, TP),
        P(),
        P(None, "rep", None, TP),
        P(None, "rep", None, TP),
        P("rep"),
        P("rep"),
        P("rep"),
        P("rep", None),
    )
    return jax.shard_map(
        layer, mesh=mesh, in_specs=placed, out_specs=P(("rep",) + TP, None), check_vma=False
    )
```
